128 devices in a mesh: leaf: 16 (over z, y), col: 8 (over x, core).
Axes of the slice: x: 4, y: 4, z: 4, core: 2. Of those that a mesh axis runs over, the one named last changes fastest.
Arguments:
- child_fronts: float32 [16, 4096, 4096], P('leaf', 'col'), may hold values from -8 to 8, as said below
- child_index: int32 [16, 14], replicated, may hold values from 0 to 47, as said below
- parent_front: float32 [12288, 12288], P('leaf', 'col'), may hold values from -8 to 8, as said below
Outputs:
- child_factor: float32 [16, 4096, 512], P('leaf', 'col')
- parent_factor: float32 [12288, 12288], P('leaf', 'col')
The draws below stay inside these ranges and needn't reach their ends.
Inputs may be any that keep to these rules, and one draw needn't show every extreme that they name: `child_index`: in each row the 14 indices are distinct and so are their groups index // 3; hence one row names at most 2 indices in any aligned group of 6 blocks (blocks 6k to 6k+5), and exactly 2 in some. `child_fronts`: each child front is symmetric with diagonal entries of 0.5 to 7 and smallest eigenvalue above 0.5. `parent_front`: symmetric with diagonal entries of 0.5 to 7 and smallest eigenvalue above 0.5.
All inputs are finite; a program needn't handle non-finite values.
Results may differ from the reference program's by a relative error of at most 0.00016.
Values sent between devices are 32-bit elements; how exact they have to be, the bound alone decides.
No kernel may reach another device: no remote copies, remote signals or barrier semaphores. Data moves between devices by JAX's collectives and lax.ppermute only.
A program may use at most 192 MiB of HBM per device.

```python
import jax
import jax.numpy as jnp
from jax import lax

B = 256
PC = 2
ROWBLK = 3
CF = 16
CC = 14
PF = 12288
CHILDREN = 16


def spd_front(key, order):
    key_factor = jax.random.fold_in(key, 0)
    key_diagonal = jax.random.fold_in(key, 2)
    factor_rank = min(order // 4, 1024)
    factor = jax.random.truncated_normal(key_factor, -4.0, 4.0, (order, factor_rank), jnp.float32)
    coupled = jnp.dot(factor, factor.T, precision=lax.Precision.HIGHEST, preferred_element_type=jnp.float32) * (1.0 / factor_rank)
    diagonal = jax.random.uniform(key_diagonal, (order,), jnp.float32, 0.5, 1.0)
    rows = lax.broadcasted_iota(jnp.int32, (order, order), 0)
    cols = lax.broadcasted_iota(jnp.int32, (order, order), 1)
    return coupled + jnp.where(rows == cols, diagonal[:, None], 0.0)


def draw_child_fronts(key, part):
    child_keys = jax.random.split(jax.random.fold_in(key, 11), CHILDREN)
    return lax.map(lambda one_key: spd_front(one_key, CF * B), child_keys)


def draw_parent_front(key, part):
    return spd_front(jax.random.fold_in(key, 13), PF)


def draw_child_index(key, part):
    base = jax.random.fold_in(key, 17)
    child_keys = jax.random.split(base, CHILDREN)
    groups = jax.vmap(lambda one_key: jax.random.permutation(one_key, CF)[:CC])(child_keys)
    offsets = jax.random.randint(jax.random.fold_in(base, 7), (CHILDREN, CC), 0, ROWBLK)
    return (groups * ROWBLK + offsets).astype(jnp.int32)


def setup_inputs(seed: int = 0) -> dict:
    arg_keys = jax.random.split(jax.random.key(seed), 4)
    return {
        "child_fronts": draw_child_fronts(jax.random.fold_in(arg_keys[3], 71), 0),
        "child_index": draw_child_index(jax.random.fold_in(arg_keys[3], 71), 0),
        "parent_front": draw_parent_front(jax.random.fold_in(arg_keys[3], 71), 0),
    }


highest = lax.Precision.HIGHEST

def partial_factor(front, width):
    pivot = jnp.linalg.cholesky(front[:width, :width])
    below = jax.scipy.linalg.solve_triangular(pivot, front[width:, :width].T, lower=True).T
    schur = front[width:, width:] - jnp.dot(below.astype(jnp.float32), below.T.astype(jnp.float32), precision=highest, preferred_element_type=jnp.float32)
    return (pivot, below, schur)

def reference(child_fronts, child_index, parent_front):
    child_width = PC * B
    offsets = jnp.arange(B, dtype=jnp.int32)
    assembled = parent_front
    factors = []
    for child in range(CHILDREN):
        pivot, below, schur = partial_factor(child_fronts[child], child_width)
        factors.append(jnp.concatenate([pivot, below], 0))
        places = (child_index[child][:, None] * B + offsets[None, :]).reshape(-1).astype(jnp.int32)
        assembled = assembled.at[places[:, None], places[None, :]].add(schur)
    width = ROWBLK * B
    pivot, below, schur = partial_factor(assembled, width)
    upper = jnp.concatenate([pivot, jnp.zeros((width, PF - width), jnp.float32)], 1)
    lower = jnp.concatenate([below, schur], 1)
    return (jnp.stack(factors), jnp.concatenate([upper, lower], 0))
```

```python
import jax
import jax.numpy as jnp
from jax import lax
from jax.sharding import PartitionSpec as P

B = 256
PC = 2
ROWBLK = 3


highest = lax.Precision.HIGHEST


def spread_2(shard, axis, root):
    mine = lax.axis_index(axis) == root
    return lax.psum(jnp.where(mine, shard, jnp.zeros_like(shard)), axis)


def solve_rows(factor, rows):
    return jax.scipy.linalg.solve_triangular(factor, rows.T, lower=True).T


def lower_inverse(factor):
    eye = jnp.eye(factor.shape[0], dtype=factor.dtype)
    return jax.scipy.linalg.solve_triangular(factor, eye, lower=True)


def route_slots(indices, col_blocks):
    target = indices // col_blocks
    count = indices.shape[-1]
    earlier_mask = lax.broadcasted_iota(jnp.int32, (count, count), 1) < lax.broadcasted_iota(
        jnp.int32, (count, count), 0
    )
    same = target[..., :, None] == target[..., None, :]
    ranking = jnp.sum((same & earlier_mask).astype(jnp.int32), axis=-1)
    return (target, ranking)


def per_device(child_fronts, child_index, parent_front):
    leaf_pos = lax.axis_index("leaf")
    col_pos = lax.axis_index("col")
    leaf_count = lax.axis_size("leaf")
    col_count = lax.axis_size("col")
    share = leaf_count // col_count
    children = child_index.shape[0]
    contrib_count = child_index.shape[1]
    front_rows = child_fronts[0]
    row_count = front_rows.shape[0]
    pivot_width = PC * B
    raw_panel = front_rows[:, :pivot_width]
    whole_panel = lax.all_gather(raw_panel, "col", axis=0, tiled=True)
    pivot_factor = jnp.linalg.cholesky(whole_panel[:pivot_width])
    pivot_inverse = lower_inverse(pivot_factor)
    solved_all = jnp.dot(
        whole_panel, pivot_inverse.T, precision=highest, preferred_element_type=jnp.float32
    )
    own_rows = lax.dynamic_slice_in_dim(solved_all, col_pos * row_count, row_count, 0)
    first_device = col_pos == 0
    child_out = jnp.where(first_device, pivot_factor, own_rows)[None]
    update_rows = front_rows[:, pivot_width:] - jnp.dot(
        own_rows, solved_all[pivot_width:].T, precision=highest, preferred_element_type=jnp.float32
    )
    update_rows = jnp.where(first_device, 0.0, update_rows)
    col_blocks = ROWBLK * leaf_count // col_count
    own_index = lax.dynamic_index_in_dim(child_index, leaf_pos, 0, keepdims=False)
    parent_pivots = ROWBLK * B
    block_rows = row_count // B
    diag = jnp.zeros((ROWBLK, B, B), jnp.float32)
    for local in range(block_rows):
        block = jnp.clip((col_pos - 1) * block_rows + local, 0, contrib_count - 1)
        piece = lax.dynamic_slice(update_rows, (local * B, block * B), (B, B))
        place = lax.dynamic_index_in_dim(own_index, block, 0, keepdims=False)
        hit = (jnp.arange(ROWBLK, dtype=jnp.int32) == place) & (col_pos >= 1)
        diag = diag + jnp.where(hit[:, None, None], piece[None], 0.0)
    diag_full = jnp.zeros((parent_pivots, parent_pivots), jnp.float32)
    for p in range(ROWBLK):
        diag_full = lax.dynamic_update_slice(diag_full, diag[p], (p * B, p * B))
    corner = (leaf_pos == 0) & (col_pos == 0)
    early = diag_full + jnp.where(corner, parent_front[:, :parent_pivots], 0.0)
    pivot_block = lax.psum(early, ("leaf", "col"))
    parent_pivot = jnp.linalg.cholesky(pivot_block)
    parent_inverse = lower_inverse(parent_pivot)
    target, ranking = route_slots(own_index, col_blocks)
    slot_ids = jnp.arange(col_count * share, dtype=jnp.int32)
    selector = (slot_ids[:, None] == (target * share + ranking)[None, :]).astype(jnp.float32)
    selector = selector.reshape(col_count, share, contrib_count)
    pieces = update_rows.reshape(row_count, contrib_count, B)
    outgoing = jnp.einsum("msc,rcb->mrsb", selector, pieces, precision=highest)
    incoming = lax.all_to_all(outgoing, "col", split_axis=0, concat_axis=0, tiled=True)
    columns = incoming.reshape(col_count * row_count, share * B)
    contrib_rows = columns[pivot_width:].reshape(contrib_count, B, share * B)
    leaf_target = own_index // ROWBLK
    row_select = (jnp.arange(leaf_count, dtype=jnp.int32)[:, None] == leaf_target[None, :]).astype(
        jnp.float32
    )
    outgoing_rows = jnp.einsum("lr,rbx->lbx", row_select, contrib_rows, precision=highest)
    arrived = lax.all_to_all(outgoing_rows, "leaf", split_axis=0, concat_axis=0, tiled=True)
    all_target, all_rank = route_slots(child_index, col_blocks)
    local_col = child_index - col_pos * col_blocks
    hits = (all_target == col_pos)[:, :, None, None]
    hits = hits & (
        all_rank[:, :, None, None] == jnp.arange(share, dtype=jnp.int32)[None, None, :, None]
    )
    hits = hits & (
        local_col[:, :, None, None] == jnp.arange(col_blocks, dtype=jnp.int32)[None, None, None, :]
    )
    col_select = jnp.sum(hits.astype(jnp.float32), axis=1)
    local_row = child_index - leaf_pos * ROWBLK
    row_place = jnp.sum(
        (local_row[:, :, None] == jnp.arange(ROWBLK, dtype=jnp.int32)[None, None, :]).astype(
            jnp.float32
        ),
        axis=1,
    )
    arrived_blocks = arrived.reshape(children, B, share, B)
    place_map = jnp.einsum("gp,gsq->gspq", row_place, col_select)
    update = jnp.einsum("gspq,gbse->pbqe", place_map, arrived_blocks, precision=highest)
    assembled = parent_front + update.reshape(ROWBLK * B, col_blocks * B)
    raw_rows = spread_2(assembled[:, :parent_pivots], "col", 0)
    received = []
    for turn in range(share):
        received.append(spread_2(raw_rows, "leaf", col_pos * share + turn))
    row_panel = jnp.dot(
        raw_rows, parent_inverse.T, precision=highest, preferred_element_type=jnp.float32
    )
    col_panel = jnp.dot(
        jnp.concatenate(received, 0),
        parent_inverse.T,
        precision=highest,
        preferred_element_type=jnp.float32,
    )
    schur = assembled - jnp.dot(
        row_panel, col_panel.T, precision=highest, preferred_element_type=jnp.float32
    )
    left = jnp.where(leaf_pos == 0, parent_pivot, row_panel)
    left_full = jnp.concatenate(
        [left, jnp.zeros((left.shape[0], assembled.shape[1] - parent_pivots), jnp.float32)], 1
    )
    global_row = leaf_pos * assembled.shape[0] + lax.broadcasted_iota(jnp.int32, assembled.shape, 0)
    global_col = col_pos * assembled.shape[1] + lax.broadcasted_iota(jnp.int32, assembled.shape, 1)
    parent_out = jnp.where(
        global_col < parent_pivots, left_full, jnp.where(global_row < parent_pivots, 0.0, schur)
    )
    return (child_out, parent_out)


def solution(mesh):
    placed = (P("leaf", "col", None), P(), P("leaf", "col"))
    return jax.shard_map(
        per_device,
        mesh=mesh,
        in_specs=placed,
        out_specs=(P("leaf", "col", None), P("leaf", "col")),
        check_vma=False,
    )
```

```python
import jax
import jax.numpy as jnp
from jax import lax
from jax.sharding import PartitionSpec as P

B = 256
PC = 2
ROWBLK = 3


highest = lax.Precision.HIGHEST


def spread_2(shard, axis, root):
    mine = lax.axis_index(axis) == root
    return lax.psum(jnp.where(mine, shard, jnp.zeros_like(shard)), axis)


def solve_rows(factor, rows):
    return jax.scipy.linalg.solve_triangular(factor, rows.T, lower=True).T


def lower_inverse(factor):
    eye = jnp.eye(factor.shape[0], dtype=factor.dtype)
    return jax.scipy.linalg.solve_triangular(factor, eye, lower=True)


def route_slots(indices, col_blocks):
    target = indices // col_blocks
    count = indices.shape[-1]
    earlier_mask = lax.broadcasted_iota(jnp.int32, (count, count), 1) < lax.broadcasted_iota(
        jnp.int32, (count, count), 0
    )
    same = target[..., :, None] == target[..., None, :]
    ranking = jnp.sum((same & earlier_mask).astype(jnp.int32), axis=-1)
    return (target, ranking)


def per_device(child_fronts, child_index, parent_front):
    leaf_pos = lax.axis_index("leaf")
    col_pos = lax.axis_index("col")
    leaf_count = lax.axis_size("leaf")
    col_count = lax.axis_size("col")
    share = leaf_count // col_count
    children = child_index.shape[0]
    contrib_count = child_index.shape[1]
    front_rows = child_fronts[0]
    row_count = front_rows.shape[0]
    pivot_width = PC * B
    raw_panel = front_rows[:, :pivot_width]
    whole_panel = lax.all_gather(raw_panel, "col", axis=0, tiled=True)
    corner = (leaf_pos == 0) & (col_pos == 0)
    parent_pivots = ROWBLK * B
    front_pivot = jnp.where(corner, parent_front[:, :parent_pivots], 0.0)
    pivot_factor = jnp.linalg.cholesky(whole_panel[:pivot_width])
    pivot_inverse = lower_inverse(pivot_factor)
    solved_all = jnp.dot(
        whole_panel, pivot_inverse.T, precision=highest, preferred_element_type=jnp.float32
    )
    own_rows = lax.dynamic_slice_in_dim(solved_all, col_pos * row_count, row_count, 0)
    first_device = col_pos == 0
    child_out = jnp.where(first_device, pivot_factor, own_rows)[None]
    update_rows = front_rows[:, pivot_width:] - jnp.dot(
        own_rows, solved_all[pivot_width:].T, precision=highest, preferred_element_type=jnp.float32
    )
    update_rows = jnp.where(first_device, 0.0, update_rows)
    col_blocks = ROWBLK * leaf_count // col_count
    own_index = lax.dynamic_index_in_dim(child_index, leaf_pos, 0, keepdims=False)
    block_rows = row_count // B
    diag = jnp.zeros((ROWBLK, B, B), jnp.float32)
    for local in range(block_rows):
        block = jnp.clip((col_pos - 1) * block_rows + local, 0, contrib_count - 1)
        source = lax.dynamic_slice(front_rows, (local * B, pivot_width + block * B), (B, B))
        solved = own_rows[local * B : (local + 1) * B]
        piece = source - jnp.dot(
            solved, solved.T, precision=highest, preferred_element_type=jnp.float32
        )
        place = lax.dynamic_index_in_dim(own_index, block, 0, keepdims=False)
        hit = (jnp.arange(ROWBLK, dtype=jnp.int32) == place) & (col_pos >= 1)
        diag = diag + jnp.where(hit[:, None, None], piece[None], 0.0)
    diag_full = front_pivot
    for p in range(ROWBLK):
        corner_block = lax.dynamic_slice(diag_full, (p * B, p * B), (B, B))
        diag_full = lax.dynamic_update_slice(diag_full, corner_block + diag[p], (p * B, p * B))
    pivot_block = lax.psum(diag_full, ("leaf", "col"))
    parent_pivot = jnp.linalg.cholesky(pivot_block)
    parent_inverse = lower_inverse(parent_pivot)
    target, ranking = route_slots(own_index, col_blocks)
    slot_ids = jnp.arange(col_count * share, dtype=jnp.int32)
    selector = (slot_ids[:, None] == (target * share + ranking)[None, :]).astype(jnp.float32)
    selector = selector.reshape(col_count, share, contrib_count)
    pieces = update_rows.reshape(row_count, contrib_count, B)
    outgoing = jnp.einsum("msc,rcb->mrsb", selector, pieces, precision=highest)
    outgoing = outgoing + pivot_block[0, 0] * 0.0
    incoming = lax.all_to_all(outgoing, "col", split_axis=0, concat_axis=0, tiled=True)
    columns = incoming.reshape(col_count * row_count, share * B)
    contrib_rows = columns[pivot_width:].reshape(contrib_count, B, share * B)
    leaf_target = own_index // ROWBLK
    row_select = (jnp.arange(leaf_count, dtype=jnp.int32)[:, None] == leaf_target[None, :]).astype(
        jnp.float32
    )
    outgoing_rows = jnp.einsum("lr,rbx->lbx", row_select, contrib_rows, precision=highest)
    outgoing_rows = outgoing_rows + parent_pivot[0, 0] * 0.0
    arrived = lax.all_to_all(outgoing_rows, "leaf", split_axis=0, concat_axis=0, tiled=True)
    all_target, all_rank = route_slots(child_index, col_blocks)
    local_col = child_index - col_pos * col_blocks
    hits = (all_target == col_pos)[:, :, None, None]
    hits = hits & (
        all_rank[:, :, None, None] == jnp.arange(share, dtype=jnp.int32)[None, None, :, None]
    )
    hits = hits & (
        local_col[:, :, None, None] == jnp.arange(col_blocks, dtype=jnp.int32)[None, None, None, :]
    )
    col_select = jnp.sum(hits.astype(jnp.float32), axis=1)
    local_row = child_index - leaf_pos * ROWBLK
    row_place = jnp.sum(
        (local_row[:, :, None] == jnp.arange(ROWBLK, dtype=jnp.int32)[None, None, :]).astype(
            jnp.float32
        ),
        axis=1,
    )
    arrived_blocks = arrived.reshape(children, B, share, B) + parent_inverse[0, 0] * 0.0
    place_map = jnp.einsum("gp,gsq->gspq", row_place, col_select)
    update = jnp.einsum("gspq,gbse->pbqe", place_map, arrived_blocks, precision=highest)
    assembled = parent_front + update.reshape(ROWBLK * B, col_blocks * B)
    raw_rows = spread_2(assembled[:, :parent_pivots], "col", 0)
    received = []
    for turn in range(share):
        received.append(spread_2(raw_rows, "leaf", col_pos * share + turn))
    row_panel = jnp.dot(
        raw_rows, parent_inverse.T, precision=highest, preferred_element_type=jnp.float32
    )
    col_panel = jnp.dot(
        jnp.concatenate(received, 0),
        parent_inverse.T,
        precision=highest,
        preferred_element_type=jnp.float32,
    )
    schur = assembled - jnp.dot(
        row_panel, col_panel.T, precision=highest, preferred_element_type=jnp.float32
    )
    left = jnp.where(leaf_pos == 0, parent_pivot, row_panel)
    left_full = jnp.concatenate(
        [left, jnp.zeros((left.shape[0], assembled.shape[1] - parent_pivots), jnp.float32)], 1
    )
    global_row = leaf_pos * assembled.shape[0] + lax.broadcasted_iota(jnp.int32, assembled.shape, 0)
    global_col = col_pos * assembled.shape[1] + lax.broadcasted_iota(jnp.int32, assembled.shape, 1)
    parent_out = jnp.where(
        global_col < parent_pivots, left_full, jnp.where(global_row < parent_pivots, 0.0, schur)
    )
    return (child_out, parent_out)


def solution(mesh):
    placed = (P("leaf", "col", None), P(), P("leaf", "col"))
    return jax.shard_map(
        per_device,
        mesh=mesh,
        in_specs=placed,
        out_specs=(P("leaf", "col", None), P("leaf", "col")),
        check_vma=False,
    )
```

```python
import jax
import jax.numpy as jnp
from jax import lax
from jax.sharding import PartitionSpec as P

B = 256
PC = 2
ROWBLK = 3


highest = lax.Precision.HIGHEST


def spread_2(shard, axis, root):
    mine = lax.axis_index(axis) == root
    return lax.psum(jnp.where(mine, shard, jnp.zeros_like(shard)), axis)


def solve_rows(factor, rows):
    return jax.scipy.linalg.solve_triangular(factor, rows.T, lower=True).T


def lower_inverse(factor):
    eye = jnp.eye(factor.shape[0], dtype=factor.dtype)
    return jax.scipy.linalg.solve_triangular(factor, eye, lower=True)


def route_slots(indices, col_blocks):
    target = indices // col_blocks
    count = indices.shape[-1]
    earlier_mask = lax.broadcasted_iota(jnp.int32, (count, count), 1) < lax.broadcasted_iota(
        jnp.int32, (count, count), 0
    )
    same = target[..., :, None] == target[..., None, :]
    ranking = jnp.sum((same & earlier_mask).astype(jnp.int32), axis=-1)
    return (target, ranking)


def per_device(child_fronts, child_index, parent_front):
    leaf_pos = lax.axis_index("leaf")
    col_pos = lax.axis_index("col")
    leaf_count = lax.axis_size("leaf")
    col_count = lax.axis_size("col")
    share = leaf_count // col_count
    children = child_index.shape[0]
    contrib_count = child_index.shape[1]
    front_rows = child_fronts[0]
    row_count = front_rows.shape[0]
    pivot_width = PC * B
    raw_panel = front_rows[:, :pivot_width]
    whole_panel = lax.all_gather(raw_panel, "col", axis=0, tiled=True)
    corner = (leaf_pos == 0) & (col_pos == 0)
    parent_pivots = ROWBLK * B
    front_pivot = jnp.where(corner, parent_front[:, :parent_pivots], 0.0)
    front_pivot = lax.psum(front_pivot + whole_panel[0, 0] * 0.0, ("leaf", "col"))
    pivot_factor = jnp.linalg.cholesky(whole_panel[:pivot_width])
    pivot_inverse = lower_inverse(pivot_factor)
    solved_all = jnp.dot(
        whole_panel, pivot_inverse.T, precision=highest, preferred_element_type=jnp.float32
    )
    own_rows = lax.dynamic_slice_in_dim(solved_all, col_pos * row_count, row_count, 0)
    first_device = col_pos == 0
    child_out = jnp.where(first_device, pivot_factor, own_rows)[None]
    update_rows = front_rows[:, pivot_width:] - jnp.dot(
        own_rows, solved_all[pivot_width:].T, precision=highest, preferred_element_type=jnp.float32
    )
    update_rows = jnp.where(first_device, 0.0, update_rows)
    col_blocks = ROWBLK * leaf_count // col_count
    own_index = lax.dynamic_index_in_dim(child_index, leaf_pos, 0, keepdims=False)
    block_rows = row_count // B
    diag = jnp.zeros((ROWBLK, B, B), jnp.float32)
    for local in range(block_rows):
        block = jnp.clip((col_pos - 1) * block_rows + local, 0, contrib_count - 1)
        source = lax.dynamic_slice(front_rows, (local * B, pivot_width + block * B), (B, B))
        solved = own_rows[local * B : (local + 1) * B]
        piece = source - jnp.dot(
            solved, solved.T, precision=highest, preferred_element_type=jnp.float32
        )
        place = lax.dynamic_index_in_dim(own_index, block, 0, keepdims=False)
        hit = (jnp.arange(ROWBLK, dtype=jnp.int32) == place) & (col_pos >= 1)
        diag = diag + jnp.where(hit[:, None, None], piece[None], 0.0)
    diag = lax.psum(diag + front_pivot[0, 0] * 0.0, ("leaf", "col"))
    pivot_block = front_pivot
    for p in range(ROWBLK):
        corner_block = lax.dynamic_slice(pivot_block, (p * B, p * B), (B, B))
        pivot_block = lax.dynamic_update_slice(pivot_block, corner_block + diag[p], (p * B, p * B))
    parent_pivot = jnp.linalg.cholesky(pivot_block)
    parent_inverse = lower_inverse(parent_pivot)
    target, ranking = route_slots(own_index, col_blocks)
    slot_ids = jnp.arange(col_count * share, dtype=jnp.int32)
    selector = (slot_ids[:, None] == (target * share + ranking)[None, :]).astype(jnp.float32)
    selector = selector.reshape(col_count, share, contrib_count)
    pieces = update_rows.reshape(row_count, contrib_count, B)
    outgoing = jnp.einsum("msc,rcb->mrsb", selector, pieces, precision=highest)
    outgoing = outgoing + diag[0, 0, 0] * 0.0
    incoming = lax.all_to_all(outgoing, "col", split_axis=0, concat_axis=0, tiled=True)
    columns = incoming.reshape(col_count * row_count, share * B)
    contrib_rows = columns[pivot_width:].reshape(contrib_count, B, share * B)
    leaf_target = own_index // ROWBLK
    row_select = (jnp.arange(leaf_count, dtype=jnp.int32)[:, None] == leaf_target[None, :]).astype(
        jnp.float32
    )
    outgoing_rows = jnp.einsum("lr,rbx->lbx", row_select, contrib_rows, precision=highest)
    outgoing_rows = outgoing_rows + parent_pivot[0, 0] * 0.0
    arrived = lax.all_to_all(outgoing_rows, "leaf", split_axis=0, concat_axis=0, tiled=True)
    all_target, all_rank = route_slots(child_index, col_blocks)
    local_col = child_index - col_pos * col_blocks
    hits = (all_target == col_pos)[:, :, None, None]
    hits = hits & (
        all_rank[:, :, None, None] == jnp.arange(share, dtype=jnp.int32)[None, None, :, None]
    )
    hits = hits & (
        local_col[:, :, None, None] == jnp.arange(col_blocks, dtype=jnp.int32)[None, None, None, :]
    )
    col_select = jnp.sum(hits.astype(jnp.float32), axis=1)
    local_row = child_index - leaf_pos * ROWBLK
    row_place = jnp.sum(
        (local_row[:, :, None] == jnp.arange(ROWBLK, dtype=jnp.int32)[None, None, :]).astype(
            jnp.float32
        ),
        axis=1,
    )
    arrived_blocks = arrived.reshape(children, B, share, B) + parent_inverse[0, 0] * 0.0
    place_map = jnp.einsum("gp,gsq->gspq", row_place, col_select)
    update = jnp.einsum("gspq,gbse->pbqe", place_map, arrived_blocks, precision=highest)
    assembled = parent_front + update.reshape(ROWBLK * B, col_blocks * B)
    raw_rows = spread_2(assembled[:, :parent_pivots], "col", 0)
    received = []
    for turn in range(share):
        received.append(spread_2(raw_rows, "leaf", col_pos * share + turn))
    row_panel = jnp.dot(
        raw_rows, parent_inverse.T, precision=highest, preferred_element_type=jnp.float32
    )
    col_panel = jnp.dot(
        jnp.concatenate(received, 0),
        parent_inverse.T,
        precision=highest,
        preferred_element_type=jnp.float32,
    )
    schur = assembled - jnp.dot(
        row_panel, col_panel.T, precision=highest, preferred_element_type=jnp.float32
    )
    left = jnp.where(leaf_pos == 0, parent_pivot, row_panel)
    left_full = jnp.concatenate(
        [left, jnp.zeros((left.shape[0], assembled.shape[1] - parent_pivots), jnp.float32)], 1
    )
    global_row = leaf_pos * assembled.shape[0] + lax.broadcasted_iota(jnp.int32, assembled.shape, 0)
    global_col = col_pos * assembled.shape[1] + lax.broadcasted_iota(jnp.int32, assembled.shape, 1)
    parent_out = jnp.where(
        global_col < parent_pivots, left_full, jnp.where(global_row < parent_pivots, 0.0, schur)
    )
    return (child_out, parent_out)


def solution(mesh):
    placed = (P("leaf", "col", None), P(), P("leaf", "col"))
    return jax.shard_map(
        per_device,
        mesh=mesh,
        in_specs=placed,
        out_specs=(P("leaf", "col", None), P("leaf", "col")),
        check_vma=False,
    )
```

```python
import jax
import jax.numpy as jnp
from jax import lax
from jax.sharding import PartitionSpec as P

B = 256
PC = 2
ROWBLK = 3


highest = lax.Precision.HIGHEST


def spread_2(shard, axis, root):
    mine = lax.axis_index(axis) == root
    return lax.psum(jnp.where(mine, shard, jnp.zeros_like(shard)), axis)


def solve_rows(factor, rows):
    return jax.scipy.linalg.solve_triangular(factor, rows.T, lower=True).T


def lower_inverse(factor):
    eye = jnp.eye(factor.shape[0], dtype=factor.dtype)
    return jax.scipy.linalg.solve_triangular(factor, eye, lower=True)


def route_slots(indices, col_blocks):
    target = indices // col_blocks
    count = indices.shape[-1]
    earlier_mask = lax.broadcasted_iota(jnp.int32, (count, count), 1) < lax.broadcasted_iota(
        jnp.int32, (count, count), 0
    )
    same = target[..., :, None] == target[..., None, :]
    ranking = jnp.sum((same & earlier_mask).astype(jnp.int32), axis=-1)
    return (target, ranking)


def per_device(child_fronts, child_index, parent_front):
    leaf_pos = lax.axis_index("leaf")
    col_pos = lax.axis_index("col")
    leaf_count = lax.axis_size("leaf")
    col_count = lax.axis_size("col")
    share = leaf_count // col_count
    children = child_index.shape[0]
    front_rows = child_fronts[0]
    row_count = front_rows.shape[0]
    pivot_width = PC * B
    raw_panel = front_rows[:, :pivot_width]
    block_rows = row_count // B
    contrib_count = child_index.shape[1]
    candidates = []
    for local in range(block_rows):
        block = jnp.clip((col_pos - 1) * block_rows + local, 0, contrib_count - 1)
        candidates.append(
            lax.dynamic_slice(front_rows, (local * B, pivot_width + block * B), (B, B))
        )
    packed = jnp.concatenate([raw_panel, jnp.concatenate(candidates, 0)], 1)
    gathered = lax.all_gather(packed, "col", axis=0, tiled=True)
    whole_panel = gathered[:, :pivot_width]
    diag_sources = gathered[:, pivot_width:]
    corner = (leaf_pos == 0) & (col_pos == 0)
    parent_pivots = ROWBLK * B
    front_pivot = jnp.where(corner, parent_front[:, :parent_pivots], 0.0)
    front_pivot = lax.psum(front_pivot + whole_panel[0, 0] * 0.0, ("leaf", "col"))
    pivot_factor = jnp.linalg.cholesky(whole_panel[:pivot_width])
    pivot_inverse = lower_inverse(pivot_factor)
    solved_all = jnp.dot(
        whole_panel, pivot_inverse.T, precision=highest, preferred_element_type=jnp.float32
    )
    own_rows = lax.dynamic_slice_in_dim(solved_all, col_pos * row_count, row_count, 0)
    first_device = col_pos == 0
    child_out = jnp.where(first_device, pivot_factor, own_rows)[None]
    update_rows = front_rows[:, pivot_width:] - jnp.dot(
        own_rows, solved_all[pivot_width:].T, precision=highest, preferred_element_type=jnp.float32
    )
    update_rows = jnp.where(first_device, 0.0, update_rows)
    col_blocks = ROWBLK * leaf_count // col_count
    own_index = lax.dynamic_index_in_dim(child_index, leaf_pos, 0, keepdims=False)
    in_group = own_index < ROWBLK
    first_hit = jnp.argmax(in_group)
    has_hit = jnp.any(in_group)
    source = lax.dynamic_slice_in_dim(diag_sources, (first_hit + PC) * B, B, 0)
    solved = lax.dynamic_slice_in_dim(solved_all, (first_hit + PC) * B, B, 0)
    piece = source - jnp.dot(solved, solved.T, precision=highest, preferred_element_type=jnp.float32)
    piece = jnp.where(has_hit, piece, 0.0) + front_pivot[0, 0] * 0.0
    pieces_all = lax.all_gather(piece, "leaf", axis=0, tiled=False)
    all_hits = child_index < ROWBLK
    all_place = jnp.sum(jnp.where(all_hits, child_index, 0), axis=1)
    all_has = jnp.any(all_hits, axis=1)
    slot_pick = (
        (all_place[:, None] == jnp.arange(ROWBLK, dtype=jnp.int32)[None, :]) & all_has[:, None]
    ).astype(jnp.float32)
    diag = jnp.einsum("gp,gab->pab", slot_pick, pieces_all, precision=highest)
    pivot_block = front_pivot
    for p in range(ROWBLK):
        corner_block = lax.dynamic_slice(pivot_block, (p * B, p * B), (B, B))
        pivot_block = lax.dynamic_update_slice(pivot_block, corner_block + diag[p], (p * B, p * B))
    parent_pivot = jnp.linalg.cholesky(pivot_block)
    parent_inverse = lower_inverse(parent_pivot)
    target, ranking = route_slots(own_index, col_blocks)
    slot_ids = jnp.arange(col_count * share, dtype=jnp.int32)
    selector = (slot_ids[:, None] == (target * share + ranking)[None, :]).astype(jnp.float32)
    selector = selector.reshape(col_count, share, contrib_count)
    pieces = update_rows.reshape(row_count, contrib_count, B)
    outgoing = jnp.einsum("msc,rcb->mrsb", selector, pieces, precision=highest)
    outgoing = outgoing + diag[0, 0, 0] * 0.0
    incoming = lax.all_to_all(outgoing, "col", split_axis=0, concat_axis=0, tiled=True)
    columns = incoming.reshape(col_count * row_count, share * B)
    contrib_rows = columns[pivot_width:].reshape(contrib_count, B, share * B)
    leaf_target = own_index // ROWBLK
    row_select = (jnp.arange(leaf_count, dtype=jnp.int32)[:, None] == leaf_target[None, :]).astype(
        jnp.float32
    )
    outgoing_rows = jnp.einsum("lr,rbx->lbx", row_select, contrib_rows, precision=highest)
    outgoing_rows = outgoing_rows + parent_pivot[0, 0] * 0.0
    arrived = lax.all_to_all(outgoing_rows, "leaf", split_axis=0, concat_axis=0, tiled=True)
    all_target, all_rank = route_slots(child_index, col_blocks)
    local_col = child_index - col_pos * col_blocks
    hits = (all_target == col_pos)[:, :, None, None]
    hits = hits & (
        all_rank[:, :, None, None] == jnp.arange(share, dtype=jnp.int32)[None, None, :, None]
    )
    hits = hits & (
        local_col[:, :, None, None] == jnp.arange(col_blocks, dtype=jnp.int32)[None, None, None, :]
    )
    col_select = jnp.sum(hits.astype(jnp.float32), axis=1)
    local_row = child_index - leaf_pos * ROWBLK
    row_place = jnp.sum(
        (local_row[:, :, None] == jnp.arange(ROWBLK, dtype=jnp.int32)[None, None, :]).astype(
            jnp.float32
        ),
        axis=1,
    )
    arrived_blocks = arrived.reshape(children, B, share, B) + parent_inverse[0, 0] * 0.0
    place_map = jnp.einsum("gp,gsq->gspq", row_place, col_select)
    update = jnp.einsum("gspq,gbse->pbqe", place_map, arrived_blocks, precision=highest)
    assembled = parent_front + update.reshape(ROWBLK * B, col_blocks * B)
    raw_rows = spread_2(assembled[:, :parent_pivots], "col", 0)
    received = []
    for turn in range(share):
        received.append(spread_2(raw_rows, "leaf", col_pos * share + turn))
    row_panel = jnp.dot(
        raw_rows, parent_inverse.T, precision=highest, preferred_element_type=jnp.float32
    )
    col_panel = jnp.dot(
        jnp.concatenate(received, 0),
        parent_inverse.T,
        precision=highest,
        preferred_element_type=jnp.float32,
    )
    schur = assembled - jnp.dot(
        row_panel, col_panel.T, precision=highest, preferred_element_type=jnp.float32
    )
    left = jnp.where(leaf_pos == 0, parent_pivot, row_panel)
    left_full = jnp.concatenate(
        [left, jnp.zeros((left.shape[0], assembled.shape[1] - parent_pivots), jnp.float32)], 1
    )
    global_row = leaf_pos * assembled.shape[0] + lax.broadcasted_iota(jnp.int32, assembled.shape, 0)
    global_col = col_pos * assembled.shape[1] + lax.broadcasted_iota(jnp.int32, assembled.shape, 1)
    parent_out = jnp.where(
        global_col < parent_pivots, left_full, jnp.where(global_row < parent_pivots, 0.0, schur)
    )
    return (child_out, parent_out)


def solution(mesh):
    placed = (P("leaf", "col", None), P(), P("leaf", "col"))
    return jax.shard_map(
        per_device,
        mesh=mesh,
        in_specs=placed,
        out_specs=(P("leaf", "col", None), P("leaf", "col")),
        check_vma=False,
    )
```

```python
import jax
import jax.numpy as jnp
from jax import lax
from jax.sharding import PartitionSpec as P

B = 256
PC = 2
ROWBLK = 3


highest = lax.Precision.HIGHEST
high = lax.Precision.HIGH


def spread_2(shard, axis, root):
    mine = lax.axis_index(axis) == root
    return lax.psum(jnp.where(mine, shard, jnp.zeros_like(shard)), axis)


def solve_rows(factor, rows):
    return jax.scipy.linalg.solve_triangular(factor, rows.T, lower=True).T


def lower_inverse(factor):
    eye = jnp.eye(factor.shape[0], dtype=factor.dtype)
    return jax.scipy.linalg.solve_triangular(factor, eye, lower=True)


def route_slots(indices, col_blocks):
    target = indices // col_blocks
    count = indices.shape[-1]
    earlier_mask = lax.broadcasted_iota(jnp.int32, (count, count), 1) < lax.broadcasted_iota(
        jnp.int32, (count, count), 0
    )
    same = target[..., :, None] == target[..., None, :]
    ranking = jnp.sum((same & earlier_mask).astype(jnp.int32), axis=-1)
    return (target, ranking)


def per_device(child_fronts, child_index, parent_front):
    leaf_pos = lax.axis_index("leaf")
    col_pos = lax.axis_index("col")
    leaf_count = lax.axis_size("leaf")
    col_count = lax.axis_size("col")
    share = leaf_count // col_count
    children = child_index.shape[0]
    front_rows = child_fronts[0]
    row_count = front_rows.shape[0]
    pivot_width = PC * B
    raw_panel = front_rows[:, :pivot_width]
    block_rows = row_count // B
    contrib_count = child_index.shape[1]
    candidates = []
    for local in range(block_rows):
        block = jnp.clip((col_pos - 1) * block_rows + local, 0, contrib_count - 1)
        candidates.append(
            lax.dynamic_slice(front_rows, (local * B, pivot_width + block * B), (B, B))
        )
    packed = jnp.concatenate([raw_panel, jnp.concatenate(candidates, 0)], 1)
    gathered = lax.all_gather(packed, "col", axis=0, tiled=True)
    whole_panel = gathered[:, :pivot_width]
    diag_sources = gathered[:, pivot_width:]
    corner = (leaf_pos == 0) & (col_pos == 0)
    parent_pivots = ROWBLK * B
    front_pivot = jnp.where(corner, parent_front[:, :parent_pivots], 0.0)
    front_pivot = lax.psum(front_pivot + whole_panel[0, 0] * 0.0, ("leaf", "col"))
    pivot_factor = jnp.linalg.cholesky(whole_panel[:pivot_width])
    pivot_inverse = lower_inverse(pivot_factor)
    solved_all = jnp.dot(
        whole_panel, pivot_inverse.T, precision=high, preferred_element_type=jnp.float32
    )
    own_rows = lax.dynamic_slice_in_dim(solved_all, col_pos * row_count, row_count, 0)
    first_device = col_pos == 0
    child_out = jnp.where(first_device, pivot_factor, own_rows)[None]
    update_rows = front_rows[:, pivot_width:] - jnp.dot(
        own_rows, solved_all[pivot_width:].T, precision=high, preferred_element_type=jnp.float32
    )
    update_rows = jnp.where(first_device, 0.0, update_rows)
    col_blocks = ROWBLK * leaf_count // col_count
    own_index = lax.dynamic_index_in_dim(child_index, leaf_pos, 0, keepdims=False)
    in_group = own_index < ROWBLK
    first_hit = jnp.argmax(in_group)
    has_hit = jnp.any(in_group)
    source = lax.dynamic_slice_in_dim(diag_sources, (first_hit + PC) * B, B, 0)
    solved = lax.dynamic_slice_in_dim(solved_all, (first_hit + PC) * B, B, 0)
    piece = source - jnp.dot(solved, solved.T, precision=highest, preferred_element_type=jnp.float32)
    piece = jnp.where(has_hit, piece, 0.0) + front_pivot[0, 0] * 0.0
    pieces_all = lax.all_gather(piece, "leaf", axis=0, tiled=False)
    all_hits = child_index < ROWBLK
    all_place = jnp.sum(jnp.where(all_hits, child_index, 0), axis=1)
    all_has = jnp.any(all_hits, axis=1)
    slot_pick = (
        (all_place[:, None] == jnp.arange(ROWBLK, dtype=jnp.int32)[None, :]) & all_has[:, None]
    ).astype(jnp.float32)
    diag = jnp.einsum("gp,gab->pab", slot_pick, pieces_all, precision=highest)
    pivot_block = front_pivot
    for p in range(ROWBLK):
        corner_block = lax.dynamic_slice(pivot_block, (p * B, p * B), (B, B))
        pivot_block = lax.dynamic_update_slice(pivot_block, corner_block + diag[p], (p * B, p * B))
    parent_pivot = jnp.linalg.cholesky(pivot_block)
    parent_inverse = lower_inverse(parent_pivot)
    target, ranking = route_slots(own_index, col_blocks)
    slot_ids = jnp.arange(col_count * share, dtype=jnp.int32)
    selector = (slot_ids[:, None] == (target * share + ranking)[None, :]).astype(jnp.float32)
    selector = selector.reshape(col_count, share, contrib_count)
    pieces = update_rows.reshape(row_count, contrib_count, B)
    outgoing = jnp.einsum("msc,rcb->mrsb", selector, pieces, precision=highest)
    outgoing = outgoing + diag[0, 0, 0] * 0.0
    incoming = lax.all_to_all(outgoing, "col", split_axis=0, concat_axis=0, tiled=True)
    columns = incoming.reshape(col_count * row_count, share * B)
    contrib_rows = columns[pivot_width:].reshape(contrib_count, B, share * B)
    leaf_target = own_index // ROWBLK
    row_select = (jnp.arange(leaf_count, dtype=jnp.int32)[:, None] == leaf_target[None, :]).astype(
        jnp.float32
    )
    outgoing_rows = jnp.einsum("lr,rbx->lbx", row_select, contrib_rows, precision=highest)
    outgoing_rows = outgoing_rows + parent_pivot[0, 0] * 0.0
    arrived = lax.all_to_all(outgoing_rows, "leaf", split_axis=0, concat_axis=0, tiled=True)
    all_target, all_rank = route_slots(child_index, col_blocks)
    local_col = child_index - col_pos * col_blocks
    hits = (all_target == col_pos)[:, :, None, None]
    hits = hits & (
        all_rank[:, :, None, None] == jnp.arange(share, dtype=jnp.int32)[None, None, :, None]
    )
    hits = hits & (
        local_col[:, :, None, None] == jnp.arange(col_blocks, dtype=jnp.int32)[None, None, None, :]
    )
    col_select = jnp.sum(hits.astype(jnp.float32), axis=1)
    local_row = child_index - leaf_pos * ROWBLK
    row_place = jnp.sum(
        (local_row[:, :, None] == jnp.arange(ROWBLK, dtype=jnp.int32)[None, None, :]).astype(
            jnp.float32
        ),
        axis=1,
    )
    arrived_blocks = arrived.reshape(children, B, share, B) + parent_inverse[0, 0] * 0.0
    place_map = jnp.einsum("gp,gsq->gspq", row_place, col_select)
    update = jnp.einsum("gspq,gbse->pbqe", place_map, arrived_blocks, precision=highest)
    assembled = parent_front + update.reshape(ROWBLK * B, col_blocks * B)
    raw_rows = spread_2(assembled[:, :parent_pivots], "col", 0)
    received = []
    for turn in range(share):
        received.append(spread_2(raw_rows, "leaf", col_pos * share + turn))
    row_panel = jnp.dot(
        raw_rows, parent_inverse.T, precision=high, preferred_element_type=jnp.float32
    )
    col_panel = jnp.dot(
        jnp.concatenate(received, 0),
        parent_inverse.T,
        precision=high,
        preferred_element_type=jnp.float32,
    )
    schur = assembled - jnp.dot(
        row_panel, col_panel.T, precision=high, preferred_element_type=jnp.float32
    )
    left = jnp.where(leaf_pos == 0, parent_pivot, row_panel)
    left_full = jnp.concatenate(
        [left, jnp.zeros((left.shape[0], assembled.shape[1] - parent_pivots), jnp.float32)], 1
    )
    global_row = leaf_pos * assembled.shape[0] + lax.broadcasted_iota(jnp.int32, assembled.shape, 0)
    global_col = col_pos * assembled.shape[1] + lax.broadcasted_iota(jnp.int32, assembled.shape, 1)
    parent_out = jnp.where(
        global_col < parent_pivots, left_full, jnp.where(global_row < parent_pivots, 0.0, schur)
    )
    return (child_out, parent_out)


def solution(mesh):
    placed = (P("leaf", "col", None), P(), P("leaf", "col"))
    return jax.shard_map(
        per_device,
        mesh=mesh,
        in_specs=placed,
        out_specs=(P("leaf", "col", None), P("leaf", "col")),
        check_vma=False,
    )
```

```python
import jax
import jax.numpy as jnp
from jax import lax
from jax.sharding import PartitionSpec as P

B = 256
PC = 2
ROWBLK = 3


highest = lax.Precision.HIGHEST
high = lax.Precision.HIGH


def spread_2(shard, axis, root):
    mine = lax.axis_index(axis) == root
    return lax.psum(jnp.where(mine, shard, jnp.zeros_like(shard)), axis)


def tree_spread(shard, axis, pos, count):
    span = 1
    while span < count:
        span *= 2
    span //= 2
    while span >= 1:
        pairs = [(i, i + span) for i in range(0, count, 2 * span) if i + span < count]
        moved = lax.ppermute(shard, axis, pairs)
        shard = jnp.where(pos % (2 * span) == span, moved, shard)
        span //= 2
    return shard


def solve_rows(factor, rows):
    return jax.scipy.linalg.solve_triangular(factor, rows.T, lower=True).T


def lower_inverse(factor):
    eye = jnp.eye(factor.shape[0], dtype=factor.dtype)
    return jax.scipy.linalg.solve_triangular(factor, eye, lower=True)


def route_slots(indices, col_blocks):
    target = indices // col_blocks
    count = indices.shape[-1]
    earlier_mask = lax.broadcasted_iota(jnp.int32, (count, count), 1) < lax.broadcasted_iota(
        jnp.int32, (count, count), 0
    )
    same = target[..., :, None] == target[..., None, :]
    ranking = jnp.sum((same & earlier_mask).astype(jnp.int32), axis=-1)
    return (target, ranking)


def per_device(child_fronts, child_index, parent_front):
    leaf_pos = lax.axis_index("leaf")
    col_pos = lax.axis_index("col")
    leaf_count = lax.axis_size("leaf")
    col_count = lax.axis_size("col")
    share = leaf_count // col_count
    children = child_index.shape[0]
    front_rows = child_fronts[0]
    row_count = front_rows.shape[0]
    pivot_width = PC * B
    raw_panel = front_rows[:, :pivot_width]
    block_rows = row_count // B
    contrib_count = child_index.shape[1]
    candidates = []
    for local in range(block_rows):
        block = jnp.clip((col_pos - 1) * block_rows + local, 0, contrib_count - 1)
        candidates.append(
            lax.dynamic_slice(front_rows, (local * B, pivot_width + block * B), (B, B))
        )
    packed = jnp.concatenate([raw_panel, jnp.concatenate(candidates, 0)], 1)
    gathered = lax.all_gather(packed, "col", axis=0, tiled=True)
    whole_panel = gathered[:, :pivot_width]
    diag_sources = gathered[:, pivot_width:]
    corner = (leaf_pos == 0) & (col_pos == 0)
    parent_pivots = ROWBLK * B
    front_pivot = jnp.where(corner, parent_front[:, :parent_pivots], 0.0)
    front_pivot = lax.psum(front_pivot + whole_panel[0, 0] * 0.0, ("leaf", "col"))
    pivot_factor = jnp.linalg.cholesky(whole_panel[:pivot_width])
    pivot_inverse = lower_inverse(pivot_factor)
    solved_all = jnp.dot(
        whole_panel, pivot_inverse.T, precision=high, preferred_element_type=jnp.float32
    )
    own_rows = lax.dynamic_slice_in_dim(solved_all, col_pos * row_count, row_count, 0)
    first_device = col_pos == 0
    child_out = jnp.where(first_device, pivot_factor, own_rows)[None]
    update_rows = front_rows[:, pivot_width:] - jnp.dot(
        own_rows, solved_all[pivot_width:].T, precision=high, preferred_element_type=jnp.float32
    )
    update_rows = jnp.where(first_device, 0.0, update_rows)
    col_blocks = ROWBLK * leaf_count // col_count
    own_index = lax.dynamic_index_in_dim(child_index, leaf_pos, 0, keepdims=False)
    in_group = own_index < ROWBLK
    first_hit = jnp.argmax(in_group)
    has_hit = jnp.any(in_group)
    source = lax.dynamic_slice_in_dim(diag_sources, (first_hit + PC) * B, B, 0)
    solved = lax.dynamic_slice_in_dim(solved_all, (first_hit + PC) * B, B, 0)
    piece = source - jnp.dot(solved, solved.T, precision=highest, preferred_element_type=jnp.float32)
    piece = jnp.where(has_hit, piece, 0.0) + front_pivot[0, 0] * 0.0
    pieces_all = lax.all_gather(piece, "leaf", axis=0, tiled=False)
    all_hits = child_index < ROWBLK
    all_place = jnp.sum(jnp.where(all_hits, child_index, 0), axis=1)
    all_has = jnp.any(all_hits, axis=1)
    slot_pick = (
        (all_place[:, None] == jnp.arange(ROWBLK, dtype=jnp.int32)[None, :]) & all_has[:, None]
    ).astype(jnp.float32)
    diag = jnp.einsum("gp,gab->pab", slot_pick, pieces_all, precision=highest)
    pivot_block = front_pivot
    for p in range(ROWBLK):
        corner_block = lax.dynamic_slice(pivot_block, (p * B, p * B), (B, B))
        pivot_block = lax.dynamic_update_slice(pivot_block, corner_block + diag[p], (p * B, p * B))
    parent_pivot = jnp.linalg.cholesky(pivot_block)
    parent_inverse = lower_inverse(parent_pivot)
    target, ranking = route_slots(own_index, col_blocks)
    slot_ids = jnp.arange(col_count * share, dtype=jnp.int32)
    selector = (slot_ids[:, None] == (target * share + ranking)[None, :]).astype(jnp.float32)
    selector = selector.reshape(col_count, share, contrib_count)
    pieces = update_rows.reshape(row_count, contrib_count, B)
    outgoing = jnp.einsum("msc,rcb->mrsb", selector, pieces, precision=highest)
    outgoing = outgoing + diag[0, 0, 0] * 0.0
    incoming = lax.all_to_all(outgoing, "col", split_axis=0, concat_axis=0, tiled=True)
    columns = incoming.reshape(col_count * row_count, share * B)
    contrib_rows = columns[pivot_width:].reshape(contrib_count, B, share * B)
    leaf_target = own_index // ROWBLK
    row_select = (jnp.arange(leaf_count, dtype=jnp.int32)[:, None] == leaf_target[None, :]).astype(
        jnp.float32
    )
    outgoing_rows = jnp.einsum("lr,rbx->lbx", row_select, contrib_rows, precision=highest)
    outgoing_rows = outgoing_rows + parent_pivot[0, 0] * 0.0
    arrived = lax.all_to_all(outgoing_rows, "leaf", split_axis=0, concat_axis=0, tiled=True)
    all_target, all_rank = route_slots(child_index, col_blocks)
    local_col = child_index - col_pos * col_blocks
    hits = (all_target == col_pos)[:, :, None, None]
    hits = hits & (
        all_rank[:, :, None, None] == jnp.arange(share, dtype=jnp.int32)[None, None, :, None]
    )
    hits = hits & (
        local_col[:, :, None, None] == jnp.arange(col_blocks, dtype=jnp.int32)[None, None, None, :]
    )
    col_select = jnp.sum(hits.astype(jnp.float32), axis=1)
    local_row = child_index - leaf_pos * ROWBLK
    row_place = jnp.sum(
        (local_row[:, :, None] == jnp.arange(ROWBLK, dtype=jnp.int32)[None, None, :]).astype(
            jnp.float32
        ),
        axis=1,
    )
    arrived_blocks = arrived.reshape(children, B, share, B) + parent_inverse[0, 0] * 0.0
    place_map = jnp.einsum("gp,gsq->gspq", row_place, col_select)
    update = jnp.einsum("gspq,gbse->pbqe", place_map, arrived_blocks, precision=highest)
    assembled = parent_front + update.reshape(ROWBLK * B, col_blocks * B)
    raw_rows = tree_spread(assembled[:, :parent_pivots], "col", col_pos, col_count)
    pivot_rows = spread_2(assembled, "leaf", 0)
    row_panel = jnp.dot(
        raw_rows, parent_inverse.T, precision=high, preferred_element_type=jnp.float32
    )
    col_panel = jnp.dot(
        pivot_rows.T,
        parent_inverse.T,
        precision=high,
        preferred_element_type=jnp.float32,
    )
    schur = assembled - jnp.dot(
        row_panel, col_panel.T, precision=high, preferred_element_type=jnp.float32
    )
    left = jnp.where(leaf_pos == 0, parent_pivot, row_panel)
    left_full = jnp.concatenate(
        [left, jnp.zeros((left.shape[0], assembled.shape[1] - parent_pivots), jnp.float32)], 1
    )
    global_row = leaf_pos * assembled.shape[0] + lax.broadcasted_iota(jnp.int32, assembled.shape, 0)
    global_col = col_pos * assembled.shape[1] + lax.broadcasted_iota(jnp.int32, assembled.shape, 1)
    parent_out = jnp.where(
        global_col < parent_pivots, left_full, jnp.where(global_row < parent_pivots, 0.0, schur)
    )
    return (child_out, parent_out)


def solution(mesh):
    placed = (P("leaf", "col", None), P(), P("leaf", "col"))
    return jax.shard_map(
        per_device,
        mesh=mesh,
        in_specs=placed,
        out_specs=(P("leaf", "col", None), P("leaf", "col")),
        check_vma=False,
    )
```

```python
import jax
import jax.numpy as jnp
from jax import lax
from jax.sharding import PartitionSpec as P

B = 256
PC = 2
ROWBLK = 3


highest = lax.Precision.HIGHEST
high = lax.Precision.HIGH


def spread_2(shard, axis, root):
    mine = lax.axis_index(axis) == root
    return lax.psum(jnp.where(mine, shard, jnp.zeros_like(shard)), axis)


def tree_spread(shard, axis, pos, count):
    span = 1
    while span < count:
        span *= 2
    span //= 2
    while span >= 1:
        pairs = [(i, i + span) for i in range(0, count, 2 * span) if i + span < count]
        moved = lax.ppermute(shard, axis, pairs)
        shard = jnp.where(pos % (2 * span) == span, moved, shard)
        span //= 2
    return shard


def solve_rows(factor, rows):
    return jax.scipy.linalg.solve_triangular(factor, rows.T, lower=True).T


def lower_inverse(factor):
    eye = jnp.eye(factor.shape[0], dtype=factor.dtype)
    return jax.scipy.linalg.solve_triangular(factor, eye, lower=True)


def route_slots(indices, col_blocks):
    target = indices // col_blocks
    count = indices.shape[-1]
    earlier_mask = lax.broadcasted_iota(jnp.int32, (count, count), 1) < lax.broadcasted_iota(
        jnp.int32, (count, count), 0
    )
    same = target[..., :, None] == target[..., None, :]
    ranking = jnp.sum((same & earlier_mask).astype(jnp.int32), axis=-1)
    return (target, ranking)


def per_device(child_fronts, child_index, parent_front):
    leaf_pos = lax.axis_index("leaf")
    col_pos = lax.axis_index("col")
    leaf_count = lax.axis_size("leaf")
    col_count = lax.axis_size("col")
    share = leaf_count // col_count
    children = child_index.shape[0]
    front_rows = child_fronts[0]
    row_count = front_rows.shape[0]
    pivot_width = PC * B
    raw_panel = front_rows[:, :pivot_width]
    block_rows = row_count // B
    contrib_count = child_index.shape[1]
    candidates = []
    for local in range(block_rows):
        block = jnp.clip((col_pos - 1) * block_rows + local, 0, contrib_count - 1)
        candidates.append(
            lax.dynamic_slice(front_rows, (local * B, pivot_width + block * B), (B, B))
        )
    packed = jnp.concatenate([raw_panel, jnp.concatenate(candidates, 0)], 1)
    gathered = lax.all_gather(packed, "col", axis=0, tiled=True)
    whole_panel = gathered[:, :pivot_width]
    diag_sources = gathered[:, pivot_width:]
    corner = (leaf_pos == 0) & (col_pos == 0)
    parent_pivots = ROWBLK * B
    front_pivot = jnp.where(corner, parent_front[:, :parent_pivots], 0.0)
    front_pivot = lax.psum(front_pivot + whole_panel[0, 0] * 0.0, ("leaf", "col"))
    pivot_factor = jnp.linalg.cholesky(whole_panel[:pivot_width])
    solved_all = solve_rows(pivot_factor, whole_panel)
    own_rows = lax.dynamic_slice_in_dim(solved_all, col_pos * row_count, row_count, 0)
    first_device = col_pos == 0
    child_out = jnp.where(first_device, pivot_factor, own_rows)[None]
    update_rows = front_rows[:, pivot_width:] - jnp.dot(
        own_rows, solved_all[pivot_width:].T, precision=high, preferred_element_type=jnp.float32
    )
    update_rows = jnp.where(first_device, 0.0, update_rows)
    col_blocks = ROWBLK * leaf_count // col_count
    own_index = lax.dynamic_index_in_dim(child_index, leaf_pos, 0, keepdims=False)
    in_group = own_index < ROWBLK
    first_hit = jnp.argmax(in_group)
    has_hit = jnp.any(in_group)
    source = lax.dynamic_slice_in_dim(diag_sources, (first_hit + PC) * B, B, 0)
    solved = lax.dynamic_slice_in_dim(solved_all, (first_hit + PC) * B, B, 0)
    piece = source - jnp.dot(solved, solved.T, precision=highest, preferred_element_type=jnp.float32)
    piece = jnp.where(has_hit, piece, 0.0) + front_pivot[0, 0] * 0.0
    pieces_all = lax.all_gather(piece, "leaf", axis=0, tiled=False)
    all_hits = child_index < ROWBLK
    all_place = jnp.sum(jnp.where(all_hits, child_index, 0), axis=1)
    all_has = jnp.any(all_hits, axis=1)
    slot_pick = (
        (all_place[:, None] == jnp.arange(ROWBLK, dtype=jnp.int32)[None, :]) & all_has[:, None]
    ).astype(jnp.float32)
    diag = jnp.einsum("gp,gab->pab", slot_pick, pieces_all, precision=highest)
    pivot_block = front_pivot
    for p in range(ROWBLK):
        corner_block = lax.dynamic_slice(pivot_block, (p * B, p * B), (B, B))
        pivot_block = lax.dynamic_update_slice(pivot_block, corner_block + diag[p], (p * B, p * B))
    parent_pivot = jnp.linalg.cholesky(pivot_block)
    parent_inverse = lower_inverse(parent_pivot)
    target, ranking = route_slots(own_index, col_blocks)
    slot_ids = jnp.arange(col_count * share, dtype=jnp.int32)
    selector = (slot_ids[:, None] == (target * share + ranking)[None, :]).astype(jnp.float32)
    selector = selector.reshape(col_count, share, contrib_count) + diag[0, 0, 0] * 0.0
    pieces = update_rows.reshape(row_count, contrib_count, B)
    outgoing = jnp.einsum("msc,rcb->mrsb", selector, pieces, precision=highest)
    incoming = lax.all_to_all(outgoing, "col", split_axis=0, concat_axis=0, tiled=True)
    columns = incoming.reshape(col_count * row_count, share * B)
    contrib_rows = columns[pivot_width:].reshape(contrib_count, B, share * B)
    leaf_target = own_index // ROWBLK
    row_select = (jnp.arange(leaf_count, dtype=jnp.int32)[:, None] == leaf_target[None, :]).astype(
        jnp.float32
    )
    row_select = row_select + parent_pivot[0, 0] * 0.0
    outgoing_rows = jnp.einsum("lr,rbx->lbx", row_select, contrib_rows, precision=highest)
    arrived = lax.all_to_all(outgoing_rows, "leaf", split_axis=0, concat_axis=0, tiled=True)
    all_target, all_rank = route_slots(child_index, col_blocks)
    local_col = child_index - col_pos * col_blocks
    hits = (all_target == col_pos)[:, :, None, None]
    hits = hits & (
        all_rank[:, :, None, None] == jnp.arange(share, dtype=jnp.int32)[None, None, :, None]
    )
    hits = hits & (
        local_col[:, :, None, None] == jnp.arange(col_blocks, dtype=jnp.int32)[None, None, None, :]
    )
    col_select = jnp.sum(hits.astype(jnp.float32), axis=1)
    local_row = child_index - leaf_pos * ROWBLK
    row_place = jnp.sum(
        (local_row[:, :, None] == jnp.arange(ROWBLK, dtype=jnp.int32)[None, None, :]).astype(
            jnp.float32
        ),
        axis=1,
    )
    arrived_blocks = arrived.reshape(children, B, share, B)
    place_map = jnp.einsum("gp,gsq->gspq", row_place, col_select) + parent_inverse[0, 0] * 0.0
    update = jnp.einsum("gspq,gbse->pbqe", place_map, arrived_blocks, precision=highest)
    assembled = parent_front + update.reshape(ROWBLK * B, col_blocks * B)
    raw_rows = tree_spread(assembled[:, :parent_pivots], "col", col_pos, col_count)
    pivot_rows = spread_2(assembled, "leaf", 0)
    row_panel = jnp.dot(
        raw_rows, parent_inverse.T, precision=high, preferred_element_type=jnp.float32
    )
    col_panel = jnp.dot(
        pivot_rows.T,
        parent_inverse.T,
        precision=high,
        preferred_element_type=jnp.float32,
    )
    schur = assembled - jnp.dot(
        row_panel, col_panel.T, precision=high, preferred_element_type=jnp.float32
    )
    left = jnp.where(leaf_pos == 0, parent_pivot, row_panel)
    left_full = jnp.concatenate(
        [left, jnp.zeros((left.shape[0], assembled.shape[1] - parent_pivots), jnp.float32)], 1
    )
    global_row = leaf_pos * assembled.shape[0] + lax.broadcasted_iota(jnp.int32, assembled.shape, 0)
    global_col = col_pos * assembled.shape[1] + lax.broadcasted_iota(jnp.int32, assembled.shape, 1)
    parent_out = jnp.where(
        global_col < parent_pivots, left_full, jnp.where(global_row < parent_pivots, 0.0, schur)
    )
    return (child_out, parent_out)


def solution(mesh):
    placed = (P("leaf", "col", None), P(), P("leaf", "col"))
    return jax.shard_map(
        per_device,
        mesh=mesh,
        in_specs=placed,
        out_specs=(P("leaf", "col", None), P("leaf", "col")),
        check_vma=False,
    )
```

```python
import jax
import jax.numpy as jnp
from jax import lax
from jax.sharding import PartitionSpec as P

B = 256
PC = 2
ROWBLK = 3


highest = lax.Precision.HIGHEST
high = lax.Precision.HIGH


def spread_2(shard, axis, root):
    mine = lax.axis_index(axis) == root
    return lax.psum(jnp.where(mine, shard, jnp.zeros_like(shard)), axis)


def tree_spread(shard, axis, pos, count):
    span = 1
    while span < count:
        span *= 2
    span //= 2
    while span >= 1:
        pairs = [(i, i + span) for i in range(0, count, 2 * span) if i + span < count]
        moved = lax.ppermute(shard, axis, pairs)
        shard = jnp.where(pos % (2 * span) == span, moved, shard)
        span //= 2
    return shard


def solve_rows(factor, rows):
    return jax.scipy.linalg.solve_triangular(factor, rows.T, lower=True).T


def lower_inverse(factor):
    eye = jnp.eye(factor.shape[0], dtype=factor.dtype)
    return jax.scipy.linalg.solve_triangular(factor, eye, lower=True)


def route_slots(indices, col_blocks):
    target = indices // col_blocks
    count = indices.shape[-1]
    earlier_mask = lax.broadcasted_iota(jnp.int32, (count, count), 1) < lax.broadcasted_iota(
        jnp.int32, (count, count), 0
    )
    same = target[..., :, None] == target[..., None, :]
    ranking = jnp.sum((same & earlier_mask).astype(jnp.int32), axis=-1)
    return (target, ranking)


def per_device(child_fronts, child_index, parent_front):
    leaf_pos = lax.axis_index("leaf")
    col_pos = lax.axis_index("col")
    leaf_count = lax.axis_size("leaf")
    col_count = lax.axis_size("col")
    share = leaf_count // col_count
    children = child_index.shape[0]
    front_rows = child_fronts[0]
    row_count = front_rows.shape[0]
    pivot_width = PC * B
    raw_panel = front_rows[:, :pivot_width]
    block_rows = row_count // B
    contrib_count = child_index.shape[1]
    candidates = []
    for local in range(block_rows):
        block = jnp.clip((col_pos - 1) * block_rows + local, 0, contrib_count - 1)
        candidates.append(
            lax.dynamic_slice(front_rows, (local * B, pivot_width + block * B), (B, B))
        )
    packed = jnp.concatenate([raw_panel, jnp.concatenate(candidates, 0)], 1)
    gathered = lax.all_gather(packed, "col", axis=0, tiled=True)
    whole_panel = gathered[:, :pivot_width]
    diag_sources = gathered[:, pivot_width:]
    corner = (leaf_pos == 0) & (col_pos == 0)
    parent_pivots = ROWBLK * B
    front_pivot = jnp.where(corner, parent_front[:, :parent_pivots], 0.0)
    front_pivot = lax.psum(front_pivot + whole_panel[0, 0] * 0.0, ("leaf", "col"))
    pivot_factor = jnp.linalg.cholesky(whole_panel[:pivot_width])
    pivot_inverse = lower_inverse(pivot_factor)
    solved_all = jnp.dot(
        whole_panel, pivot_inverse.T, precision=high, preferred_element_type=jnp.float32
    )
    own_rows = lax.dynamic_slice_in_dim(solved_all, col_pos * row_count, row_count, 0)
    first_device = col_pos == 0
    child_out = jnp.where(first_device, pivot_factor, own_rows)[None]
    update_rows = front_rows[:, pivot_width:] - jnp.dot(
        own_rows, solved_all[pivot_width:].T, precision=high, preferred_element_type=jnp.float32
    )
    update_rows = jnp.where(first_device, 0.0, update_rows)
    col_blocks = ROWBLK * leaf_count // col_count
    own_index = lax.dynamic_index_in_dim(child_index, leaf_pos, 0, keepdims=False)
    in_group = own_index < ROWBLK
    first_hit = jnp.argmax(in_group)
    has_hit = jnp.any(in_group)
    source = lax.dynamic_slice_in_dim(diag_sources, (first_hit + PC) * B, B, 0)
    solved = lax.dynamic_slice_in_dim(solved_all, (first_hit + PC) * B, B, 0)
    piece = source - jnp.dot(solved, solved.T, precision=highest, preferred_element_type=jnp.float32)
    piece = jnp.where(has_hit, piece, 0.0) + front_pivot[0, 0] * 0.0
    pieces_all = lax.all_gather(piece, "leaf", axis=0, tiled=False)
    all_hits = child_index < ROWBLK
    all_place = jnp.sum(jnp.where(all_hits, child_index, 0), axis=1)
    all_has = jnp.any(all_hits, axis=1)
    slot_pick = (
        (all_place[:, None] == jnp.arange(ROWBLK, dtype=jnp.int32)[None, :]) & all_has[:, None]
    ).astype(jnp.float32)
    diag = jnp.einsum("gp,gab->pab", slot_pick, pieces_all, precision=highest)
    pivot_block = front_pivot
    for p in range(ROWBLK):
        corner_block = lax.dynamic_slice(pivot_block, (p * B, p * B), (B, B))
        pivot_block = lax.dynamic_update_slice(pivot_block, corner_block + diag[p], (p * B, p * B))
    parent_pivot = jnp.linalg.cholesky(pivot_block)
    parent_inverse = lower_inverse(parent_pivot)
    target, ranking = route_slots(own_index, col_blocks)
    slot_ids = jnp.arange(col_count * share, dtype=jnp.int32)
    selector = (slot_ids[:, None] == (target * share + ranking)[None, :]).astype(jnp.float32)
    selector = selector.reshape(col_count, share, contrib_count) + diag[0, 0, 0] * 0.0
    pieces = update_rows.reshape(row_count, contrib_count, B)
    outgoing = jnp.einsum("msc,rcb->mrsb", selector, pieces, precision=highest)
    incoming = lax.all_to_all(outgoing, "col", split_axis=0, concat_axis=0, tiled=True)
    columns = incoming.reshape(col_count * row_count, share * B)
    contrib_rows = columns[pivot_width:].reshape(contrib_count, B, share * B)
    leaf_target = own_index // ROWBLK
    row_select = (jnp.arange(leaf_count, dtype=jnp.int32)[:, None] == leaf_target[None, :]).astype(
        jnp.float32
    )
    row_select = row_select + parent_pivot[0, 0] * 0.0
    outgoing_rows = jnp.einsum("lr,rbx->lbx", row_select, contrib_rows, precision=highest)
    arrived = lax.all_to_all(outgoing_rows, "leaf", split_axis=0, concat_axis=0, tiled=True)
    all_target, all_rank = route_slots(child_index, col_blocks)
    local_col = child_index - col_pos * col_blocks
    hits = (all_target == col_pos)[:, :, None, None]
    hits = hits & (
        all_rank[:, :, None, None] == jnp.arange(share, dtype=jnp.int32)[None, None, :, None]
    )
    hits = hits & (
        local_col[:, :, None, None] == jnp.arange(col_blocks, dtype=jnp.int32)[None, None, None, :]
    )
    col_select = jnp.sum(hits.astype(jnp.float32), axis=1)
    local_row = child_index - leaf_pos * ROWBLK
    row_place = jnp.sum(
        (local_row[:, :, None] == jnp.arange(ROWBLK, dtype=jnp.int32)[None, None, :]).astype(
            jnp.float32
        ),
        axis=1,
    )
    arrived_blocks = arrived.reshape(children, B, share, B)
    place_map = jnp.einsum("gp,gsq->gspq", row_place, col_select) + parent_inverse[0, 0] * 0.0
    update = jnp.einsum("gspq,gbse->pbqe", place_map, arrived_blocks, precision=highest)
    assembled = parent_front + update.reshape(ROWBLK * B, col_blocks * B)
    raw_rows = tree_spread(assembled[:, :parent_pivots], "col", col_pos, col_count)
    pivot_rows = spread_2(assembled, "leaf", 0)
    row_panel = jnp.dot(
        raw_rows, parent_inverse.T, precision=high, preferred_element_type=jnp.float32
    )
    col_panel = jnp.dot(
        pivot_rows.T,
        parent_inverse.T,
        precision=high,
        preferred_element_type=jnp.float32,
    )
    schur = assembled - jnp.dot(
        row_panel, col_panel.T, precision=high, preferred_element_type=jnp.float32
    )
    left = jnp.where(leaf_pos == 0, parent_pivot, row_panel)
    left_full = jnp.concatenate(
        [left, jnp.zeros((left.shape[0], assembled.shape[1] - parent_pivots), jnp.float32)], 1
    )
    global_row = leaf_pos * assembled.shape[0] + lax.broadcasted_iota(jnp.int32, assembled.shape, 0)
    global_col = col_pos * assembled.shape[1] + lax.broadcasted_iota(jnp.int32, assembled.shape, 1)
    parent_out = jnp.where(
        global_col < parent_pivots, left_full, jnp.where(global_row < parent_pivots, 0.0, schur)
    )
    return (child_out, parent_out)


def solution(mesh):
    placed = (P("leaf", "col", None), P(), P("leaf", "col"))
    return jax.shard_map(
        per_device,
        mesh=mesh,
        in_specs=placed,
        out_specs=(P("leaf", "col", None), P("leaf", "col")),
        check_vma=False,
    )
```

```python
import jax
import jax.numpy as jnp
from jax import lax
from jax.sharding import PartitionSpec as P

B = 256
PC = 2
ROWBLK = 3


highest = lax.Precision.HIGHEST
high = lax.Precision.HIGH


def spread_2(shard, axis, root):
    mine = lax.axis_index(axis) == root
    return lax.psum(jnp.where(mine, shard, jnp.zeros_like(shard)), axis)


def tree_spread(shard, axis, pos, count):
    span = 1
    while span < count:
        span *= 2
    span //= 2
    while span >= 1:
        pairs = [(i, i + span) for i in range(0, count, 2 * span) if i + span < count]
        moved = lax.ppermute(shard, axis, pairs)
        shard = jnp.where(pos % (2 * span) == span, moved, shard)
        span //= 2
    return shard


def solve_rows(factor, rows):
    return jax.scipy.linalg.solve_triangular(factor, rows.T, lower=True).T


def lower_inverse(factor):
    eye = jnp.eye(factor.shape[0], dtype=factor.dtype)
    return jax.scipy.linalg.solve_triangular(factor, eye, lower=True)


def route_slots(indices, col_blocks):
    target = indices // col_blocks
    count = indices.shape[-1]
    earlier_mask = lax.broadcasted_iota(jnp.int32, (count, count), 1) < lax.broadcasted_iota(
        jnp.int32, (count, count), 0
    )
    same = target[..., :, None] == target[..., None, :]
    ranking = jnp.sum((same & earlier_mask).astype(jnp.int32), axis=-1)
    return (target, ranking)


def per_device(child_fronts, child_index, parent_front):
    leaf_pos = lax.axis_index("leaf")
    col_pos = lax.axis_index("col")
    leaf_count = lax.axis_size("leaf")
    col_count = lax.axis_size("col")
    share = leaf_count // col_count
    children = child_index.shape[0]
    front_rows = child_fronts[0]
    row_count = front_rows.shape[0]
    pivot_width = PC * B
    raw_panel = front_rows[:, :pivot_width]
    block_rows = row_count // B
    contrib_count = child_index.shape[1]
    candidates = []
    for local in range(block_rows):
        block = jnp.clip((col_pos - 1) * block_rows + local, 0, contrib_count - 1)
        candidates.append(
            lax.dynamic_slice(front_rows, (local * B, pivot_width + block * B), (B, B))
        )
    packed = jnp.concatenate([raw_panel, jnp.concatenate(candidates, 0)], 1)
    gathered = lax.all_gather(packed, "col", axis=0, tiled=True)
    whole_panel = gathered[:, :pivot_width]
    diag_sources = gathered[:, pivot_width:]
    corner = (leaf_pos == 0) & (col_pos == 0)
    parent_pivots = ROWBLK * B
    front_pivot = jnp.where(corner, parent_front[:, :parent_pivots], 0.0)
    front_pivot = tree_spread(front_pivot, "leaf", leaf_pos, leaf_count)
    front_pivot = tree_spread(front_pivot, "col", col_pos, col_count)
    pivot_factor = jnp.linalg.cholesky(whole_panel[:pivot_width])
    pivot_inverse = lower_inverse(pivot_factor)
    solved_all = jnp.dot(
        whole_panel, pivot_inverse.T, precision=high, preferred_element_type=jnp.float32
    )
    own_rows = lax.dynamic_slice_in_dim(solved_all, col_pos * row_count, row_count, 0)
    first_device = col_pos == 0
    child_out = jnp.where(first_device, pivot_factor, own_rows)[None]
    update_rows = front_rows[:, pivot_width:] - jnp.dot(
        own_rows, solved_all[pivot_width:].T, precision=high, preferred_element_type=jnp.float32
    )
    update_rows = jnp.where(first_device, 0.0, update_rows)
    col_blocks = ROWBLK * leaf_count // col_count
    own_index = lax.dynamic_index_in_dim(child_index, leaf_pos, 0, keepdims=False)
    in_group = own_index < ROWBLK
    first_hit = jnp.argmax(in_group)
    has_hit = jnp.any(in_group)
    source = lax.dynamic_slice_in_dim(diag_sources, (first_hit + PC) * B, B, 0)
    solved = lax.dynamic_slice_in_dim(solved_all, (first_hit + PC) * B, B, 0)
    piece = source - jnp.dot(solved, solved.T, precision=highest, preferred_element_type=jnp.float32)
    piece = jnp.where(has_hit, piece, 0.0)
    pieces_all = lax.all_gather(piece, "leaf", axis=0, tiled=False)
    all_hits = child_index < ROWBLK
    all_place = jnp.sum(jnp.where(all_hits, child_index, 0), axis=1)
    all_has = jnp.any(all_hits, axis=1)
    slot_pick = (
        (all_place[:, None] == jnp.arange(ROWBLK, dtype=jnp.int32)[None, :]) & all_has[:, None]
    ).astype(jnp.float32)
    diag = jnp.einsum("gp,gab->pab", slot_pick, pieces_all, precision=highest)
    pivot_block = front_pivot
    for p in range(ROWBLK):
        corner_block = lax.dynamic_slice(pivot_block, (p * B, p * B), (B, B))
        pivot_block = lax.dynamic_update_slice(pivot_block, corner_block + diag[p], (p * B, p * B))
    parent_pivot = jnp.linalg.cholesky(pivot_block)
    parent_inverse = lower_inverse(parent_pivot)
    target, ranking = route_slots(own_index, col_blocks)
    slot_ids = jnp.arange(col_count * share, dtype=jnp.int32)
    selector = (slot_ids[:, None] == (target * share + ranking)[None, :]).astype(jnp.float32)
    selector = selector.reshape(col_count, share, contrib_count) + diag[0, 0, 0] * 0.0
    pieces = update_rows.reshape(row_count, contrib_count, B)
    outgoing = jnp.einsum("msc,rcb->mrsb", selector, pieces, precision=highest)
    incoming = lax.all_to_all(outgoing, "col", split_axis=0, concat_axis=0, tiled=True)
    columns = incoming.reshape(col_count * row_count, share * B)
    contrib_rows = columns[pivot_width:].reshape(contrib_count, B, share * B)
    leaf_target = own_index // ROWBLK
    row_select = (jnp.arange(leaf_count, dtype=jnp.int32)[:, None] == leaf_target[None, :]).astype(
        jnp.float32
    )
    row_select = row_select + parent_pivot[0, 0] * 0.0
    outgoing_rows = jnp.einsum("lr,rbx->lbx", row_select, contrib_rows, precision=highest)
    arrived = lax.all_to_all(outgoing_rows, "leaf", split_axis=0, concat_axis=0, tiled=True)
    all_target, all_rank = route_slots(child_index, col_blocks)
    local_col = child_index - col_pos * col_blocks
    hits = (all_target == col_pos)[:, :, None, None]
    hits = hits & (
        all_rank[:, :, None, None] == jnp.arange(share, dtype=jnp.int32)[None, None, :, None]
    )
    hits = hits & (
        local_col[:, :, None, None] == jnp.arange(col_blocks, dtype=jnp.int32)[None, None, None, :]
    )
    col_select = jnp.sum(hits.astype(jnp.float32), axis=1)
    local_row = child_index - leaf_pos * ROWBLK
    row_place = jnp.sum(
        (local_row[:, :, None] == jnp.arange(ROWBLK, dtype=jnp.int32)[None, None, :]).astype(
            jnp.float32
        ),
        axis=1,
    )
    arrived_blocks = arrived.reshape(children, B, share, B)
    place_map = jnp.einsum("gp,gsq->gspq", row_place, col_select) + parent_inverse[0, 0] * 0.0
    update = jnp.einsum("gspq,gbse->pbqe", place_map, arrived_blocks, precision=highest)
    assembled = parent_front + update.reshape(ROWBLK * B, col_blocks * B)
    raw_rows = tree_spread(assembled[:, :parent_pivots], "col", col_pos, col_count)
    pivot_rows = spread_2(assembled, "leaf", 0)
    row_panel = jnp.dot(
        raw_rows, parent_inverse.T, precision=high, preferred_element_type=jnp.float32
    )
    col_panel = jnp.dot(
        pivot_rows.T,
        parent_inverse.T,
        precision=high,
        preferred_element_type=jnp.float32,
    )
    schur = assembled - jnp.dot(
        row_panel, col_panel.T, precision=high, preferred_element_type=jnp.float32
    )
    left = jnp.where(leaf_pos == 0, parent_pivot, row_panel)
    left_full = jnp.concatenate(
        [left, jnp.zeros((left.shape[0], assembled.shape[1] - parent_pivots), jnp.float32)], 1
    )
    global_row = leaf_pos * assembled.shape[0] + lax.broadcasted_iota(jnp.int32, assembled.shape, 0)
    global_col = col_pos * assembled.shape[1] + lax.broadcasted_iota(jnp.int32, assembled.shape, 1)
    parent_out = jnp.where(
        global_col < parent_pivots, left_full, jnp.where(global_row < parent_pivots, 0.0, schur)
    )
    return (child_out, parent_out)


def solution(mesh):
    placed = (P("leaf", "col", None), P(), P("leaf", "col"))
    return jax.shard_map(
        per_device,
        mesh=mesh,
        in_specs=placed,
        out_specs=(P("leaf", "col", None), P("leaf", "col")),
        check_vma=False,
    )
```
